256 devices in a mesh: lat: 16 (over z, y_hi), lon: 16 (over y_lo, x, core).
Axes of the slice: x: 4, y: 4 (y_hi: 2, y_lo: 2; y = y_hi * 2 + y_lo), z: 8, core: 2. Of those that a mesh axis runs over, the one named last changes fastest.
Arguments:
- meridian_slab_data: bfloat16 [512, 96, 4096], P('lat', None, 'lon'), may hold values from -6 to 6
- smoothing_filter_taps: bfloat16 [3, 3, 96, 128], replicated, may hold values from -0.21875 to 0.21875
- smoothing_offset_entries: float32 [128], replicated, may hold values from -3 to 3
- opening_coarsen_taps: bfloat16 [4, 4, 128, 256], replicated, may hold values from -0.125 to 0.125
- opening_coarsen_offset: float32 [256], replicated, may hold values from -3 to 3
- closing_coarsen_taps: bfloat16 [4, 4, 256, 256], replicated, may hold values from -0.09375 to 0.09375
- closing_coarsen_offset: float32 [256], replicated, may hold values from -3 to 3
- layernorm_multiplier: float32 [256], replicated, may hold values from 0.25 to 1.75
- triple_mapping_matrix: bfloat16 [256, 768], replicated, may hold values from -0.375 to 0.375
- logit_sharpness: float32 [8], replicated, may hold values from 2.5 to 40, as said below
- mixing_return_matrix: bfloat16 [256, 256], replicated, may hold values from -0.375 to 0.375
Outputs:
- encoded: bfloat16 [128, 1024, 256], P('lat', 'lon')
The draws below stay inside these ranges and needn't reach their ends.
Inputs may be any that keep to these rules, and one draw needn't show every extreme that they name: `logit_sharpness`: per-head score scales.
All inputs are finite; a program needn't handle non-finite values.
Results may differ from the reference program's by a relative error of at most 0.034.
Values may be sent and summed in bfloat16 or wider, within the bound.
No kernel may reach another device: no remote copies, remote signals or barrier semaphores. Data moves between devices by JAX's collectives and lax.ppermute only.
A program may use at most 128 MiB of HBM per device.

```python
import jax
import jax.numpy as jnp
from jax import lax

CIN = 96
PRIMARY_CHANS = 128
REDUCED_CHANS = 256
HEADS = 8
LAT = 512
LON = 4096


def draw_logit_sharpness(key, part):
    base = jax.random.uniform(key, (HEADS,), jnp.float32, 2.5, 8.0)
    return base


def level_of(stream_key, dims, shards, least, largest):
    gain = 1.0
    for position, parts in shards:
        draws = jax.random.uniform(jax.random.fold_in(jax.random.fold_in(stream_key, 6), position), (parts,), jnp.float32, least / len(shards), largest / len(shards))
        gain = gain * jnp.repeat(jnp.exp(draws), dims[position] // parts).reshape((-1,) + (1,) * (len(dims) - 1 - position))
    return gain


def scatter_about(key, shape, scale, bound, pieces=(), kind=jnp.bfloat16):
    entries = jax.random.normal(key, shape, jnp.float32) * scale
    if len(pieces) > 0:
        entries = level_of(key, shape, pieces, -0.22, 0.18) * entries
    return jnp.clip(entries, min=-bound, max=bound).astype(kind)


def setup_inputs(seed: int = 0) -> dict:
    keys = jax.random.split(jax.random.key(seed), 12)
    return {
        "meridian_slab_data": scatter_about(keys[0], (LAT, CIN, LON), 1.0, 6.0, ((0, 16), (2, 16))),
        "smoothing_filter_taps": scatter_about(keys[1], (3, 3, CIN, PRIMARY_CHANS), (9 * CIN) ** -0.5, 0.21875),
        "smoothing_offset_entries": scatter_about(keys[2], (PRIMARY_CHANS,), 0.5, 3.0, (), jnp.float32),
        "opening_coarsen_taps": scatter_about(keys[3], (4, 4, PRIMARY_CHANS, REDUCED_CHANS), (16 * PRIMARY_CHANS) ** -0.5, 0.125),
        "opening_coarsen_offset": scatter_about(keys[4], (REDUCED_CHANS,), 0.5, 3.0, (), jnp.float32),
        "closing_coarsen_taps": scatter_about(keys[5], (4, 4, REDUCED_CHANS, REDUCED_CHANS), (16 * REDUCED_CHANS) ** -0.5, 0.09375),
        "closing_coarsen_offset": scatter_about(keys[6], (REDUCED_CHANS,), 0.5, 3.0, (), jnp.float32),
        "layernorm_multiplier": jnp.clip(1.0 + 0.15 * jax.random.normal(keys[7], (REDUCED_CHANS,), jnp.float32), 0.25, 1.75),
        "triple_mapping_matrix": scatter_about(keys[8], (REDUCED_CHANS, 3 * REDUCED_CHANS), REDUCED_CHANS ** -0.5, 0.375),
        "logit_sharpness": draw_logit_sharpness(jax.random.fold_in(keys[11], 71), 0),
        "mixing_return_matrix": scatter_about(keys[10], (REDUCED_CHANS, REDUCED_CHANS), REDUCED_CHANS ** -0.5, 0.375),
    }


def pad_grid(values):
    wrapped = jnp.concatenate([values[:, -1:], values, values[:, :1]], axis=1)
    return jnp.pad(wrapped, ((1, 1), (0, 0), (0, 0)))

def apply_filter(values, kernel, bias, stride):
    padded = pad_grid(values).astype(jnp.float32)
    total = lax.conv_general_dilated(padded[None], kernel.astype(jnp.float32), (stride, stride), 'VALID', dimension_numbers=('NHWC', 'HWIO', 'NHWC'), precision=lax.Precision.HIGHEST)[0]
    return jax.nn.silu(total + bias).astype(jnp.bfloat16)

def reference(meridian_slab_data, smoothing_filter_taps, smoothing_offset_entries, opening_coarsen_taps, opening_coarsen_offset, closing_coarsen_taps, closing_coarsen_offset, layernorm_multiplier, triple_mapping_matrix, logit_sharpness, mixing_return_matrix):
    channels_last = jnp.transpose(meridian_slab_data, (0, 2, 1))
    opening_halved = apply_filter(channels_last, smoothing_filter_taps, smoothing_offset_entries, 1)
    closing_halved = apply_filter(opening_halved, opening_coarsen_taps, opening_coarsen_offset, 2)
    activation_maps = apply_filter(closing_halved, closing_coarsen_taps, closing_coarsen_offset, 2)
    widths = activation_maps.shape[2]
    per_group_channel_count = widths // HEADS
    upcast = activation_maps.astype(jnp.float32)
    mean = lax.optimization_barrier(jnp.mean(upcast, axis=-1, keepdims=True))
    centred = upcast - mean
    variance = lax.optimization_barrier(jnp.mean(centred * centred, axis=-1, keepdims=True))
    normed = (centred * lax.rsqrt(variance + 1e-05) * layernorm_multiplier).astype(jnp.bfloat16)
    projected = jnp.einsum('rtc,cf->rtf', normed.astype(jnp.float32), triple_mapping_matrix.astype(jnp.float32), precision=lax.Precision.HIGHEST)
    shape = (activation_maps.shape[0], activation_maps.shape[1], HEADS, per_group_channel_count)
    logit_multiplier = (logit_sharpness / jnp.sqrt(jnp.float32(per_group_channel_count)))[:, None]
    query = (projected[..., :widths].reshape(shape) * logit_multiplier).astype(jnp.bfloat16)
    key = projected[..., widths:2 * widths].reshape(shape).astype(jnp.bfloat16)
    value = projected[..., 2 * widths:].reshape(shape).astype(jnp.bfloat16)

    def one_row(trio):
        row_query, row_key, row_value = trio
        scores = jnp.einsum('shd,thd->hst', row_query.astype(jnp.float32), row_key.astype(jnp.float32), precision=lax.Precision.HIGHEST)
        best = lax.optimization_barrier(jnp.max(scores, axis=-1, keepdims=True))
        weights = jnp.exp(scores - best)
        total = lax.optimization_barrier(jnp.sum(weights, axis=-1))
        rounded = weights.astype(jnp.bfloat16).astype(jnp.float32)
        summed = jnp.einsum('hst,thd->shd', rounded, row_value.astype(jnp.float32), precision=lax.Precision.HIGHEST)
        return (summed / jnp.transpose(total)[:, :, None]).astype(jnp.bfloat16)
    attended = lax.map(one_row, (query, key, value)).reshape(activation_maps.shape)
    mixed = jnp.einsum('rtc,cf->rtf', attended.astype(jnp.float32), mixing_return_matrix.astype(jnp.float32), precision=lax.Precision.HIGHEST)
    return (upcast + mixed).astype(jnp.bfloat16)
```

```python
import jax
import jax.numpy as jnp
from jax import lax
from jax.sharding import PartitionSpec as P

HEADS = 8
HALO = 4


def extend_lat(value, width):
    size, length = lax.axis_size("lat"), value.shape[0]
    up = [(i, i + 1) for i in range(size - 1)]
    down = [(i + 1, i) for i in range(size - 1)]
    before = lax.ppermute(value[length - width :], "lat", up)
    after = lax.ppermute(value[:width], "lat", down)
    return jnp.concatenate([before, value, after], axis=0)


def extend_lon(value, width, dim):
    size, length = lax.axis_size("lon"), value.shape[dim]
    up = [(i, (i + 1) % size) for i in range(size)]
    down = [(j, i) for i, j in up]
    last = lax.slice_in_dim(value, length - width, length, axis=dim)
    initial = lax.slice_in_dim(value, 0, width, axis=dim)
    before = lax.ppermute(last, "lon", up)
    after = lax.ppermute(initial, "lon", down)
    return jnp.concatenate([before, value, after], axis=dim)


def clear_outside(value, start, total):
    count = value.shape[0]
    rows = start + jnp.arange(count)
    keep = (rows >= 0) & (rows < total)
    shape = (count,) + (1,) * (value.ndim - 1)
    return jnp.where(keep.reshape(shape), value, jnp.zeros_like(value))


def first_conv(extended, kernel, bias):
    total = lax.conv_general_dilated(
        extended[None],
        kernel,
        (1, 1),
        "VALID",
        dimension_numbers=("NHCW", "HWIO", "NHWC"),
        preferred_element_type=jnp.float32,
    )[0]
    return jax.nn.silu(total + bias).astype(jnp.bfloat16)


def halving_filter(extended, kernel, bias):
    total = lax.conv_general_dilated(
        extended[None],
        kernel,
        (2, 2),
        "VALID",
        dimension_numbers=("NHWC", "HWIO", "NHWC"),
        preferred_element_type=jnp.float32,
    )[0]
    return jax.nn.silu(total + bias).astype(jnp.bfloat16)


def on_device(
    meridian_slab_data,
    smoothing_filter_taps,
    smoothing_offset_entries,
    opening_coarsen_taps,
    opening_coarsen_offset,
    closing_coarsen_taps,
    closing_coarsen_offset,
    layernorm_multiplier,
    triple_mapping_matrix,
    logit_sharpness,
    mixing_return_matrix,
):
    band = meridian_slab_data.shape[0]
    lat_total = band * lax.axis_size("lat")
    base = lax.axis_index("lat") * band
    extended = extend_lat(meridian_slab_data, HALO)
    extended = extend_lon(extended, HALO, 2)
    opening_halved = first_conv(extended, smoothing_filter_taps, smoothing_offset_entries)
    opening_halved = clear_outside(opening_halved, base - HALO + 1, lat_total)
    closing_halved = halving_filter(opening_halved, opening_coarsen_taps, opening_coarsen_offset)
    closing_halved = clear_outside(closing_halved, base // 2 - 1, lat_total // 2)
    closing_halved = lax.optimization_barrier(closing_halved)
    activation_maps = halving_filter(
        closing_halved, closing_coarsen_taps, closing_coarsen_offset
    )
    rows, tokens, widths = activation_maps.shape
    per_group_channel_count = widths // HEADS
    upcast = activation_maps.astype(jnp.float32)
    mean = jnp.mean(upcast, axis=-1, keepdims=True)
    centred = upcast - mean
    variance = jnp.mean(centred * centred, axis=-1, keepdims=True)
    normed = (centred * lax.rsqrt(variance + 1e-05) * layernorm_multiplier).astype(jnp.bfloat16)
    projected = jnp.dot(normed, triple_mapping_matrix, preferred_element_type=jnp.float32)
    shape = (rows, tokens, HEADS, per_group_channel_count)
    logit_multiplier = (logit_sharpness / jnp.sqrt(jnp.float32(per_group_channel_count)))[:, None]
    query = (projected[..., :widths].reshape(shape) * logit_multiplier).astype(jnp.bfloat16)
    key = projected[..., widths : 2 * widths].reshape(shape).astype(jnp.bfloat16)
    value = projected[..., 2 * widths :].reshape(shape).astype(jnp.bfloat16)

    sectors = lax.axis_size("lon")
    items = rows * HEADS
    per_device = items // sectors
    trio = jnp.concatenate([query, key, value], axis=-1)
    trio = jnp.transpose(trio, (0, 2, 1, 3)).reshape(sectors, per_device, tokens, 3 * per_group_channel_count)
    trio = lax.all_to_all(trio, "lon", 0, 0, tiled=True)
    trio = jnp.transpose(trio, (1, 0, 2, 3)).reshape(per_device, sectors * tokens, 3 * per_group_channel_count)
    q_items = trio[..., :per_group_channel_count]
    k_items = trio[..., per_group_channel_count : 2 * per_group_channel_count]
    v_items = trio[..., 2 * per_group_channel_count :]
    scores = jnp.einsum("isd,itd->ist", q_items, k_items, preferred_element_type=jnp.float32)
    best = jnp.max(scores, axis=-1, keepdims=True)
    weights = jnp.exp(scores - best)
    total = jnp.sum(weights, axis=-1, keepdims=True)
    summed = jnp.einsum(
        "ist,itd->isd", weights.astype(jnp.bfloat16), v_items, preferred_element_type=jnp.float32
    )
    attended = (summed / total).astype(jnp.bfloat16)
    attended = attended.reshape(per_device, sectors, tokens, per_group_channel_count)
    attended = jnp.transpose(attended, (1, 0, 2, 3))
    attended = lax.all_to_all(attended, "lon", 0, 0, tiled=True)
    attended = attended.reshape(rows, HEADS, tokens, per_group_channel_count)
    joined = jnp.transpose(attended, (0, 2, 1, 3)).reshape(rows, tokens, widths)
    mixed_out = jnp.dot(joined, mixing_return_matrix, preferred_element_type=jnp.float32)
    return (upcast + mixed_out).astype(jnp.bfloat16)


def solution(mesh):
    return jax.shard_map(
        on_device,
        mesh=mesh,
        in_specs=(P("lat", None, "lon"), P(), P(), P(), P(), P(), P(), P(), P(), P(), P()),
        out_specs=P("lat", "lon", None),
        check_vma=False,
    )
```

```python
import jax
import jax.numpy as jnp
from jax import lax
from jax.sharding import PartitionSpec as P

HEADS = 8
HALO = 4


def extend_lat(value, width):
    size, length = lax.axis_size("lat"), value.shape[0]
    up = [(i, i + 1) for i in range(size - 1)]
    down = [(i + 1, i) for i in range(size - 1)]
    before = lax.ppermute(value[length - width :], "lat", up)
    after = lax.ppermute(value[:width], "lat", down)
    return jnp.concatenate([before, value, after], axis=0)


def extend_lon(value, width, dim):
    size, length = lax.axis_size("lon"), value.shape[dim]
    up = [(i, (i + 1) % size) for i in range(size)]
    down = [(j, i) for i, j in up]
    last = lax.slice_in_dim(value, length - width, length, axis=dim)
    initial = lax.slice_in_dim(value, 0, width, axis=dim)
    before = lax.ppermute(last, "lon", up)
    after = lax.ppermute(initial, "lon", down)
    return jnp.concatenate([before, value, after], axis=dim)


def clear_outside(value, start, total):
    count = value.shape[0]
    rows = start + jnp.arange(count)
    keep = (rows >= 0) & (rows < total)
    shape = (count,) + (1,) * (value.ndim - 1)
    return jnp.where(keep.reshape(shape), value, jnp.zeros_like(value))


def first_conv(extended, kernel, bias):
    total = lax.conv_general_dilated(
        extended[None],
        kernel,
        (1, 1),
        "VALID",
        dimension_numbers=("NHCW", "HWIO", "NHWC"),
        preferred_element_type=jnp.float32,
    )[0]
    return jax.nn.silu(total + bias).astype(jnp.bfloat16)


def halving_filter(extended, kernel, bias):
    total = lax.conv_general_dilated(
        extended[None],
        kernel,
        (2, 2),
        "VALID",
        dimension_numbers=("NHWC", "HWIO", "NHWC"),
        preferred_element_type=jnp.float32,
    )[0]
    return jax.nn.silu(total + bias).astype(jnp.bfloat16)


def on_device(
    meridian_slab_data,
    smoothing_filter_taps,
    smoothing_offset_entries,
    opening_coarsen_taps,
    opening_coarsen_offset,
    closing_coarsen_taps,
    closing_coarsen_offset,
    layernorm_multiplier,
    triple_mapping_matrix,
    logit_sharpness,
    mixing_return_matrix,
):
    band = meridian_slab_data.shape[0]
    lat_total = band * lax.axis_size("lat")
    base = lax.axis_index("lat") * band
    extended = extend_lat(meridian_slab_data, HALO)
    extended = extend_lon(extended, HALO, 2)
    opening_halved = first_conv(extended, smoothing_filter_taps, smoothing_offset_entries)
    opening_halved = clear_outside(opening_halved, base - HALO + 1, lat_total)
    closing_halved = halving_filter(opening_halved, opening_coarsen_taps, opening_coarsen_offset)
    closing_halved = clear_outside(closing_halved, base // 2 - 1, lat_total // 2)
    closing_halved = lax.optimization_barrier(closing_halved)
    activation_maps = halving_filter(
        closing_halved, closing_coarsen_taps, closing_coarsen_offset
    )
    rows, tokens, widths = activation_maps.shape
    per_group_channel_count = widths // HEADS
    upcast = activation_maps.astype(jnp.float32)
    mean = jnp.mean(upcast, axis=-1, keepdims=True)
    centred = upcast - mean
    variance = jnp.mean(centred * centred, axis=-1, keepdims=True)
    normed = (centred * lax.rsqrt(variance + 1e-05) * layernorm_multiplier).astype(jnp.bfloat16)
    d = widths // HEADS
    logit_multiplier = logit_sharpness / jnp.sqrt(jnp.float32(d))

    sectors = lax.axis_size("lon")
    per_row = sectors // rows
    heads_here = HEADS // per_row
    half = lax.axis_index("lon") % per_row
    row_copies = jnp.repeat(normed, per_row, axis=0)
    gathered = lax.all_to_all(row_copies, "lon", 0, 0, tiled=True)
    row_tokens = gathered.reshape(sectors * tokens, widths)
    mapping = triple_mapping_matrix.reshape(widths, 3, HEADS, d)
    mapping = lax.dynamic_slice_in_dim(mapping, half * heads_here, heads_here, axis=2)
    projected = jnp.einsum("tc,cjhd->jhtd", row_tokens, mapping, preferred_element_type=jnp.float32)
    multiplier = lax.dynamic_slice_in_dim(logit_multiplier, half * heads_here, heads_here)
    q_items = (projected[0] * multiplier[:, None, None]).astype(jnp.bfloat16)
    k_items = projected[1].astype(jnp.bfloat16)
    v_items = projected[2].astype(jnp.bfloat16)
    per_device = heads_here
    scores = jnp.einsum("isd,itd->ist", q_items, k_items, preferred_element_type=jnp.float32)
    best = jnp.max(scores, axis=-1, keepdims=True)
    weights = jnp.exp(scores - best)
    total = jnp.sum(weights, axis=-1, keepdims=True)
    summed = jnp.einsum(
        "ist,itd->isd", weights.astype(jnp.bfloat16), v_items, preferred_element_type=jnp.float32
    )
    attended = (summed / total).astype(jnp.bfloat16)
    attended = attended.reshape(per_device, sectors, tokens, per_group_channel_count)
    attended = jnp.transpose(attended, (1, 0, 2, 3))
    attended = lax.all_to_all(attended, "lon", 0, 0, tiled=True)
    attended = attended.reshape(rows, HEADS, tokens, per_group_channel_count)
    joined = jnp.transpose(attended, (0, 2, 1, 3)).reshape(rows, tokens, widths)
    mixed_out = jnp.dot(joined, mixing_return_matrix, preferred_element_type=jnp.float32)
    return (upcast + mixed_out).astype(jnp.bfloat16)


def solution(mesh):
    return jax.shard_map(
        on_device,
        mesh=mesh,
        in_specs=(P("lat", None, "lon"), P(), P(), P(), P(), P(), P(), P(), P(), P(), P()),
        out_specs=P("lat", "lon", None),
        check_vma=False,
    )
```

```python
import jax
import jax.numpy as jnp
from jax import lax
from jax.sharding import PartitionSpec as P

HEADS = 8
HALO = 4


def extend_lat(value, width):
    size, length = lax.axis_size("lat"), value.shape[0]
    up = [(i, i + 1) for i in range(size - 1)]
    down = [(i + 1, i) for i in range(size - 1)]
    before = lax.ppermute(value[length - width :], "lat", up)
    after = lax.ppermute(value[:width], "lat", down)
    return jnp.concatenate([before, value, after], axis=0)


def extend_lon(value, width, dim):
    size, length = lax.axis_size("lon"), value.shape[dim]
    up = [(i, (i + 1) % size) for i in range(size)]
    down = [(j, i) for i, j in up]
    last = lax.slice_in_dim(value, length - width, length, axis=dim)
    initial = lax.slice_in_dim(value, 0, width, axis=dim)
    before = lax.ppermute(last, "lon", up)
    after = lax.ppermute(initial, "lon", down)
    return jnp.concatenate([before, value, after], axis=dim)


def extend_both(value, width):
    n_lat, n_lon = lax.axis_size("lat"), lax.axis_size("lon")
    h, w = value.shape[0], value.shape[2]

    def shifted(piece, da, db):
        pairs = []
        for a in range(n_lat):
            if 0 <= a + da < n_lat:
                for b in range(n_lon):
                    pairs.append((a * n_lon + b, (a + da) * n_lon + (b + db) % n_lon))
        return lax.ppermute(piece, ("lat", "lon"), pairs)

    low_rows, high_rows = value[h - width :], value[:width]
    top = lax.ppermute(low_rows, "lat", [(i, i + 1) for i in range(n_lat - 1)])
    bottom = lax.ppermute(high_rows, "lat", [(i + 1, i) for i in range(n_lat - 1)])
    left = lax.ppermute(value[:, :, w - width :], "lon", [(i, (i + 1) % n_lon) for i in range(n_lon)])
    right = lax.ppermute(value[:, :, :width], "lon", [((i + 1) % n_lon, i) for i in range(n_lon)])
    top_left = shifted(low_rows[:, :, w - width :], 1, 1)
    top_right = shifted(low_rows[:, :, :width], 1, -1)
    bottom_left = shifted(high_rows[:, :, w - width :], -1, 1)
    bottom_right = shifted(high_rows[:, :, :width], -1, -1)
    return jnp.concatenate(
        [
            jnp.concatenate([top_left, top, top_right], axis=2),
            jnp.concatenate([left, value, right], axis=2),
            jnp.concatenate([bottom_left, bottom, bottom_right], axis=2),
        ],
        axis=0,
    )


def clear_outside(value, start, total):
    count = value.shape[0]
    rows = start + jnp.arange(count)
    keep = (rows >= 0) & (rows < total)
    shape = (count,) + (1,) * (value.ndim - 1)
    return jnp.where(keep.reshape(shape), value, jnp.zeros_like(value))


def first_conv(extended, kernel, bias):
    total = lax.conv_general_dilated(
        extended[None],
        kernel,
        (1, 1),
        "VALID",
        dimension_numbers=("NHCW", "HWIO", "NHWC"),
        preferred_element_type=jnp.float32,
    )[0]
    return jax.nn.silu(total + bias).astype(jnp.bfloat16)


def halving_filter(extended, kernel, bias):
    total = lax.conv_general_dilated(
        extended[None],
        kernel,
        (2, 2),
        "VALID",
        dimension_numbers=("NHWC", "HWIO", "NHWC"),
        preferred_element_type=jnp.float32,
    )[0]
    return jax.nn.silu(total + bias).astype(jnp.bfloat16)


def on_device(
    meridian_slab_data,
    smoothing_filter_taps,
    smoothing_offset_entries,
    opening_coarsen_taps,
    opening_coarsen_offset,
    closing_coarsen_taps,
    closing_coarsen_offset,
    layernorm_multiplier,
    triple_mapping_matrix,
    logit_sharpness,
    mixing_return_matrix,
):
    band = meridian_slab_data.shape[0]
    lat_total = band * lax.axis_size("lat")
    base = lax.axis_index("lat") * band
    extended = extend_both(meridian_slab_data, HALO)
    opening_halved = first_conv(extended, smoothing_filter_taps, smoothing_offset_entries)
    opening_halved = clear_outside(opening_halved, base - HALO + 1, lat_total)
    closing_halved = halving_filter(opening_halved, opening_coarsen_taps, opening_coarsen_offset)
    closing_halved = clear_outside(closing_halved, base // 2 - 1, lat_total // 2)
    closing_halved = lax.optimization_barrier(closing_halved)
    activation_maps = halving_filter(
        closing_halved, closing_coarsen_taps, closing_coarsen_offset
    )
    rows, tokens, widths = activation_maps.shape
    per_group_channel_count = widths // HEADS
    upcast = activation_maps.astype(jnp.float32)
    mean = jnp.mean(upcast, axis=-1, keepdims=True)
    centred = upcast - mean
    variance = jnp.mean(centred * centred, axis=-1, keepdims=True)
    normed = (centred * lax.rsqrt(variance + 1e-05) * layernorm_multiplier).astype(jnp.bfloat16)
    d = widths // HEADS
    logit_multiplier = logit_sharpness / jnp.sqrt(jnp.float32(d))

    sectors = lax.axis_size("lon")
    per_row = sectors // rows
    heads_here = HEADS // per_row
    half = lax.axis_index("lon") % per_row
    row_copies = jnp.repeat(normed, per_row, axis=0)
    gathered = lax.all_to_all(row_copies, "lon", 0, 0, tiled=True)
    row_tokens = gathered.reshape(sectors * tokens, widths)
    mapping = triple_mapping_matrix.reshape(widths, 3, HEADS, d)
    mapping = lax.dynamic_slice_in_dim(mapping, half * heads_here, heads_here, axis=2)
    projected = jnp.einsum("tc,cjhd->jhtd", row_tokens, mapping, preferred_element_type=jnp.float32)
    multiplier = lax.dynamic_slice_in_dim(logit_multiplier, half * heads_here, heads_here)
    q_items = (projected[0] * multiplier[:, None, None]).astype(jnp.bfloat16)
    k_items = projected[1].astype(jnp.bfloat16)
    v_items = projected[2].astype(jnp.bfloat16)
    per_device = heads_here
    scores = jnp.einsum("isd,itd->ist", q_items, k_items, preferred_element_type=jnp.float32)
    best = jnp.max(scores, axis=-1, keepdims=True)
    weights = jnp.exp(scores - best)
    total = jnp.sum(weights, axis=-1, keepdims=True)
    summed = jnp.einsum(
        "ist,itd->isd", weights.astype(jnp.bfloat16), v_items, preferred_element_type=jnp.float32
    )
    attended = (summed / total).astype(jnp.bfloat16)
    attended = attended.reshape(per_device, sectors, tokens, per_group_channel_count)
    attended = jnp.transpose(attended, (1, 0, 2, 3))
    attended = lax.all_to_all(attended, "lon", 0, 0, tiled=True)
    attended = attended.reshape(rows, HEADS, tokens, per_group_channel_count)
    joined = jnp.transpose(attended, (0, 2, 1, 3)).reshape(rows, tokens, widths)
    mixed_out = jnp.dot(joined, mixing_return_matrix, preferred_element_type=jnp.float32)
    return (upcast + mixed_out).astype(jnp.bfloat16)


def solution(mesh):
    return jax.shard_map(
        on_device,
        mesh=mesh,
        in_specs=(P("lat", None, "lon"), P(), P(), P(), P(), P(), P(), P(), P(), P(), P()),
        out_specs=P("lat", "lon", None),
        check_vma=False,
    )
```

```python
import jax
import jax.numpy as jnp
from jax import lax
from jax.sharding import PartitionSpec as P

HEADS = 8
HALO = 4


def extend_lat(value, width):
    size, length = lax.axis_size("lat"), value.shape[0]
    up = [(i, i + 1) for i in range(size - 1)]
    down = [(i + 1, i) for i in range(size - 1)]
    source = lax.optimization_barrier(value)
    before = lax.ppermute(source[length - width :], "lat", up)
    after = lax.ppermute(source[:width], "lat", down)
    return jnp.concatenate([before, value, after], axis=0)


def extend_lon(value, width, dim):
    size, length = lax.axis_size("lon"), value.shape[dim]
    up = [(i, (i + 1) % size) for i in range(size)]
    down = [(j, i) for i, j in up]
    last = lax.slice_in_dim(value, length - width, length, axis=dim)
    initial = lax.slice_in_dim(value, 0, width, axis=dim)
    before = lax.ppermute(last, "lon", up)
    after = lax.ppermute(initial, "lon", down)
    return jnp.concatenate([before, value, after], axis=dim)


def clear_outside(value, start, total):
    count = value.shape[0]
    rows = start + jnp.arange(count)
    keep = (rows >= 0) & (rows < total)
    shape = (count,) + (1,) * (value.ndim - 1)
    return jnp.where(keep.reshape(shape), value, jnp.zeros_like(value))


def first_conv(extended, kernel, bias):
    total = lax.conv_general_dilated(
        extended[None],
        kernel,
        (1, 1),
        "VALID",
        dimension_numbers=("NHCW", "HWIO", "NHWC"),
        preferred_element_type=jnp.float32,
    )[0]
    return jax.nn.silu(total + bias).astype(jnp.bfloat16)


def halving_filter(extended, kernel, bias):
    total = lax.conv_general_dilated(
        extended[None],
        kernel,
        (2, 2),
        "VALID",
        dimension_numbers=("NHWC", "HWIO", "NHWC"),
        preferred_element_type=jnp.float32,
    )[0]
    return jax.nn.silu(total + bias).astype(jnp.bfloat16)


def on_device(
    meridian_slab_data,
    smoothing_filter_taps,
    smoothing_offset_entries,
    opening_coarsen_taps,
    opening_coarsen_offset,
    closing_coarsen_taps,
    closing_coarsen_offset,
    layernorm_multiplier,
    triple_mapping_matrix,
    logit_sharpness,
    mixing_return_matrix,
):
    band = meridian_slab_data.shape[0]
    lat_total = band * lax.axis_size("lat")
    base = lax.axis_index("lat") * band
    extended = extend_lat(meridian_slab_data, HALO)
    extended = extend_lon(extended, HALO, 2)
    opening_halved = first_conv(extended, smoothing_filter_taps, smoothing_offset_entries)
    opening_halved = clear_outside(opening_halved, base - HALO + 1, lat_total)
    closing_halved = halving_filter(opening_halved, opening_coarsen_taps, opening_coarsen_offset)
    closing_halved = clear_outside(closing_halved, base // 2 - 1, lat_total // 2)
    closing_halved = lax.optimization_barrier(closing_halved)
    activation_maps = halving_filter(
        closing_halved, closing_coarsen_taps, closing_coarsen_offset
    )
    rows, tokens, widths = activation_maps.shape
    per_group_channel_count = widths // HEADS
    upcast = activation_maps.astype(jnp.float32)
    mean = jnp.mean(upcast, axis=-1, keepdims=True)
    centred = upcast - mean
    variance = jnp.mean(centred * centred, axis=-1, keepdims=True)
    normed = (centred * lax.rsqrt(variance + 1e-05) * layernorm_multiplier).astype(jnp.bfloat16)
    d = widths // HEADS
    logit_multiplier = logit_sharpness / jnp.sqrt(jnp.float32(d))

    sectors = lax.axis_size("lon")
    per_row = sectors // rows
    heads_here = HEADS // per_row
    half = lax.axis_index("lon") % per_row
    row_copies = jnp.repeat(normed, per_row, axis=0)
    gathered = lax.all_to_all(row_copies, "lon", 0, 0, tiled=True)
    row_tokens = gathered.reshape(sectors * tokens, widths)
    mapping = triple_mapping_matrix.reshape(widths, 3, HEADS, d)
    mapping = lax.dynamic_slice_in_dim(mapping, half * heads_here, heads_here, axis=2)
    projected = jnp.einsum("tc,cjhd->jhtd", row_tokens, mapping, preferred_element_type=jnp.float32)
    multiplier = lax.dynamic_slice_in_dim(logit_multiplier, half * heads_here, heads_here)
    q_items = (projected[0] * multiplier[:, None, None]).astype(jnp.bfloat16)
    k_items = projected[1].astype(jnp.bfloat16)
    v_items = projected[2].astype(jnp.bfloat16)
    per_device = heads_here
    scores = jnp.einsum("isd,itd->ist", q_items, k_items, preferred_element_type=jnp.float32)
    best = jnp.max(scores, axis=-1, keepdims=True)
    weights = jnp.exp(scores - best)
    total = jnp.sum(weights, axis=-1, keepdims=True)
    summed = jnp.einsum(
        "ist,itd->isd", weights.astype(jnp.bfloat16), v_items, preferred_element_type=jnp.float32
    )
    attended = (summed / total).astype(jnp.bfloat16)
    attended = attended.reshape(per_device, sectors, tokens, per_group_channel_count)
    attended = jnp.transpose(attended, (1, 0, 2, 3))
    attended = lax.all_to_all(attended, "lon", 0, 0, tiled=True)
    attended = attended.reshape(rows, HEADS, tokens, per_group_channel_count)
    joined = jnp.transpose(attended, (0, 2, 1, 3)).reshape(rows, tokens, widths)
    mixed_out = jnp.dot(joined, mixing_return_matrix, preferred_element_type=jnp.float32)
    return (upcast + mixed_out).astype(jnp.bfloat16)


def solution(mesh):
    return jax.shard_map(
        on_device,
        mesh=mesh,
        in_specs=(P("lat", None, "lon"), P(), P(), P(), P(), P(), P(), P(), P(), P(), P()),
        out_specs=P("lat", "lon", None),
        check_vma=False,
    )
```

```python
import jax
import jax.numpy as jnp
from jax import lax
from jax.experimental import pallas as pl
from jax.sharding import PartitionSpec as P

HEADS = 8
HALO = 4


def extend_lat(value, width):
    size, length = lax.axis_size("lat"), value.shape[0]
    up = [(i, i + 1) for i in range(size - 1)]
    down = [(i + 1, i) for i in range(size - 1)]
    source = lax.optimization_barrier(value)
    before = lax.ppermute(source[length - width :], "lat", up)
    after = lax.ppermute(source[:width], "lat", down)
    return jnp.concatenate([before, value, after], axis=0)


def extend_lon(value, width, dim):
    size, length = lax.axis_size("lon"), value.shape[dim]
    up = [(i, (i + 1) % size) for i in range(size)]
    down = [(j, i) for i, j in up]
    last = lax.slice_in_dim(value, length - width, length, axis=dim)
    initial = lax.slice_in_dim(value, 0, width, axis=dim)
    before = lax.ppermute(last, "lon", up)
    after = lax.ppermute(initial, "lon", down)
    return jnp.concatenate([before, value, after], axis=dim)


def clear_outside(value, start, total):
    count = value.shape[0]
    rows = start + jnp.arange(count)
    keep = (rows >= 0) & (rows < total)
    shape = (count,) + (1,) * (value.ndim - 1)
    return jnp.where(keep.reshape(shape), value, jnp.zeros_like(value))


def attention_block(q_ref, k_ref, v_ref, o_ref):
    scores = lax.dot_general(
        q_ref[0], k_ref[0], (((1,), (1,)), ((), ())), preferred_element_type=jnp.float32
    )
    best = jnp.max(scores, axis=-1, keepdims=True)
    weights = jnp.exp(scores - best)
    total = jnp.sum(weights, axis=-1, keepdims=True)
    summed = jnp.dot(weights.astype(jnp.bfloat16), v_ref[0], preferred_element_type=jnp.float32)
    o_ref[0] = (summed / total).astype(o_ref.dtype)


def attend(q, k, v, block=256):
    heads, length, d = q.shape
    return pl.pallas_call(
        attention_block,
        grid=(heads, length // block),
        in_specs=[
            pl.BlockSpec((1, block, d), lambda h, i: (h, i, 0)),
            pl.BlockSpec((1, length, d), lambda h, i: (h, 0, 0)),
            pl.BlockSpec((1, length, d), lambda h, i: (h, 0, 0)),
        ],
        out_specs=pl.BlockSpec((1, block, d), lambda h, i: (h, i, 0)),
        out_shape=jax.ShapeDtypeStruct(q.shape, jnp.bfloat16),
    )(q, k, v)


def first_conv(extended, kernel, bias):
    total = lax.conv_general_dilated(
        extended[None],
        kernel,
        (1, 1),
        "VALID",
        dimension_numbers=("NHCW", "HWIO", "NHWC"),
        preferred_element_type=jnp.float32,
    )[0]
    return jax.nn.silu(total + bias).astype(jnp.bfloat16)


def halving_filter(extended, kernel, bias):
    total = lax.conv_general_dilated(
        extended[None],
        kernel,
        (2, 2),
        "VALID",
        dimension_numbers=("NHWC", "HWIO", "NHWC"),
        preferred_element_type=jnp.float32,
    )[0]
    return jax.nn.silu(total + bias).astype(jnp.bfloat16)


def on_device(
    meridian_slab_data,
    smoothing_filter_taps,
    smoothing_offset_entries,
    opening_coarsen_taps,
    opening_coarsen_offset,
    closing_coarsen_taps,
    closing_coarsen_offset,
    layernorm_multiplier,
    triple_mapping_matrix,
    logit_sharpness,
    mixing_return_matrix,
):
    band = meridian_slab_data.shape[0]
    lat_total = band * lax.axis_size("lat")
    base = lax.axis_index("lat") * band
    extended = extend_lat(meridian_slab_data, HALO)
    extended = extend_lon(extended, HALO, 2)
    opening_halved = first_conv(extended, smoothing_filter_taps, smoothing_offset_entries)
    opening_halved = clear_outside(opening_halved, base - HALO + 1, lat_total)
    closing_halved = halving_filter(opening_halved, opening_coarsen_taps, opening_coarsen_offset)
    closing_halved = clear_outside(closing_halved, base // 2 - 1, lat_total // 2)
    closing_halved = lax.optimization_barrier(closing_halved)
    activation_maps = halving_filter(
        closing_halved, closing_coarsen_taps, closing_coarsen_offset
    )
    rows, tokens, widths = activation_maps.shape
    per_group_channel_count = widths // HEADS
    upcast = activation_maps.astype(jnp.float32)
    mean = jnp.mean(upcast, axis=-1, keepdims=True)
    centred = upcast - mean
    variance = jnp.mean(centred * centred, axis=-1, keepdims=True)
    normed = (centred * lax.rsqrt(variance + 1e-05) * layernorm_multiplier).astype(jnp.bfloat16)
    d = widths // HEADS
    logit_multiplier = logit_sharpness / jnp.sqrt(jnp.float32(d))

    sectors = lax.axis_size("lon")
    per_row = sectors // rows
    heads_here = HEADS // per_row
    half = lax.axis_index("lon") % per_row
    row_copies = jnp.repeat(normed, per_row, axis=0)
    gathered = lax.all_to_all(row_copies, "lon", 0, 0, tiled=True)
    row_tokens = gathered.reshape(sectors * tokens, widths)
    mapping = triple_mapping_matrix.reshape(widths, 3, HEADS, d)
    mapping = lax.dynamic_slice_in_dim(mapping, half * heads_here, heads_here, axis=2)
    projected = jnp.einsum("tc,cjhd->jhtd", row_tokens, mapping, preferred_element_type=jnp.float32)
    multiplier = lax.dynamic_slice_in_dim(logit_multiplier, half * heads_here, heads_here)
    q_items = (projected[0] * multiplier[:, None, None]).astype(jnp.bfloat16)
    k_items = projected[1].astype(jnp.bfloat16)
    v_items = projected[2].astype(jnp.bfloat16)
    per_device = heads_here
    attended = attend(q_items, k_items, v_items)
    attended = attended.reshape(per_device, sectors, tokens, per_group_channel_count)
    attended = jnp.transpose(attended, (1, 0, 2, 3))
    attended = lax.all_to_all(attended, "lon", 0, 0, tiled=True)
    attended = attended.reshape(rows, HEADS, tokens, per_group_channel_count)
    joined = jnp.transpose(attended, (0, 2, 1, 3)).reshape(rows, tokens, widths)
    mixed_out = jnp.dot(joined, mixing_return_matrix, preferred_element_type=jnp.float32)
    return (upcast + mixed_out).astype(jnp.bfloat16)


def solution(mesh):
    return jax.shard_map(
        on_device,
        mesh=mesh,
        in_specs=(P("lat", None, "lon"), P(), P(), P(), P(), P(), P(), P(), P(), P(), P()),
        out_specs=P("lat", "lon", None),
        check_vma=False,
    )
```

```python
import jax
import jax.numpy as jnp
from jax import lax
from jax.experimental import pallas as pl
from jax.sharding import PartitionSpec as P

HEADS = 8
HALO = 4


def extend_lat(value, width):
    size, length = lax.axis_size("lat"), value.shape[0]
    up = [(i, i + 1) for i in range(size - 1)]
    down = [(i + 1, i) for i in range(size - 1)]
    source = lax.optimization_barrier(value)
    before = lax.ppermute(source[length - width :], "lat", up)
    after = lax.ppermute(source[:width], "lat", down)
    return jnp.concatenate([before, value, after], axis=0)


def extend_lon(value, width, dim):
    size, length = lax.axis_size("lon"), value.shape[dim]
    up = [(i, (i + 1) % size) for i in range(size)]
    down = [(j, i) for i, j in up]
    last = lax.slice_in_dim(value, length - width, length, axis=dim)
    initial = lax.slice_in_dim(value, 0, width, axis=dim)
    before = lax.ppermute(last, "lon", up)
    after = lax.ppermute(initial, "lon", down)
    return jnp.concatenate([before, value, after], axis=dim)


def clear_outside(value, start, total):
    count = value.shape[0]
    rows = start + jnp.arange(count)
    keep = (rows >= 0) & (rows < total)
    shape = (count,) + (1,) * (value.ndim - 1)
    return jnp.where(keep.reshape(shape), value, jnp.zeros_like(value))


def attention_block(q_ref, k_ref, v_ref, o_ref):
    scores = lax.dot_general(
        k_ref[0], q_ref[0], (((1,), (1,)), ((), ())), preferred_element_type=jnp.float32
    )
    best = jnp.max(scores, axis=0, keepdims=True)
    weights = jnp.exp(scores - best)
    total = jnp.sum(weights, axis=0, keepdims=True)
    summed = lax.dot_general(
        v_ref[0], weights.astype(jnp.bfloat16), (((0,), (0,)), ((), ())),
        preferred_element_type=jnp.float32,
    )
    o_ref[0] = (summed / total).astype(o_ref.dtype)


def attend(q, k, v, block=256):
    heads, length, d = q.shape
    out = pl.pallas_call(
        attention_block,
        grid=(heads, length // block),
        in_specs=[
            pl.BlockSpec((1, block, d), lambda h, i: (h, i, 0)),
            pl.BlockSpec((1, length, d), lambda h, i: (h, 0, 0)),
            pl.BlockSpec((1, length, d), lambda h, i: (h, 0, 0)),
        ],
        out_specs=pl.BlockSpec((1, d, block), lambda h, i: (h, 0, i)),
        out_shape=jax.ShapeDtypeStruct((heads, d, length), jnp.bfloat16),
    )(q, k, v)
    return jnp.transpose(out, (0, 2, 1))


def first_conv(extended, kernel, bias):
    total = lax.conv_general_dilated(
        extended[None],
        kernel,
        (1, 1),
        "VALID",
        dimension_numbers=("NHCW", "HWIO", "NHWC"),
        preferred_element_type=jnp.float32,
    )[0]
    return jax.nn.silu(total + bias).astype(jnp.bfloat16)


def halving_filter(extended, kernel, bias):
    total = lax.conv_general_dilated(
        extended[None],
        kernel,
        (2, 2),
        "VALID",
        dimension_numbers=("NHWC", "HWIO", "NHWC"),
        preferred_element_type=jnp.float32,
    )[0]
    return jax.nn.silu(total + bias).astype(jnp.bfloat16)


def on_device(
    meridian_slab_data,
    smoothing_filter_taps,
    smoothing_offset_entries,
    opening_coarsen_taps,
    opening_coarsen_offset,
    closing_coarsen_taps,
    closing_coarsen_offset,
    layernorm_multiplier,
    triple_mapping_matrix,
    logit_sharpness,
    mixing_return_matrix,
):
    band = meridian_slab_data.shape[0]
    lat_total = band * lax.axis_size("lat")
    base = lax.axis_index("lat") * band
    extended = extend_lat(meridian_slab_data, HALO)
    extended = extend_lon(extended, HALO, 2)
    opening_halved = first_conv(extended, smoothing_filter_taps, smoothing_offset_entries)
    opening_halved = clear_outside(opening_halved, base - HALO + 1, lat_total)
    closing_halved = halving_filter(opening_halved, opening_coarsen_taps, opening_coarsen_offset)
    closing_halved = clear_outside(closing_halved, base // 2 - 1, lat_total // 2)
    closing_halved = lax.optimization_barrier(closing_halved)
    activation_maps = halving_filter(
        closing_halved, closing_coarsen_taps, closing_coarsen_offset
    )
    rows, tokens, widths = activation_maps.shape
    per_group_channel_count = widths // HEADS
    upcast = activation_maps.astype(jnp.float32)
    mean = jnp.mean(upcast, axis=-1, keepdims=True)
    centred = upcast - mean
    variance = jnp.mean(centred * centred, axis=-1, keepdims=True)
    normed = (centred * lax.rsqrt(variance + 1e-05) * layernorm_multiplier).astype(jnp.bfloat16)
    d = widths // HEADS
    logit_multiplier = logit_sharpness / jnp.sqrt(jnp.float32(d))

    sectors = lax.axis_size("lon")
    per_row = sectors // rows
    heads_here = HEADS // per_row
    half = lax.axis_index("lon") % per_row
    row_copies = jnp.repeat(normed, per_row, axis=0)
    gathered = lax.all_to_all(row_copies, "lon", 0, 0, tiled=True)
    row_tokens = gathered.reshape(sectors * tokens, widths)
    mapping = triple_mapping_matrix.reshape(widths, 3, HEADS, d)
    mapping = lax.dynamic_slice_in_dim(mapping, half * heads_here, heads_here, axis=2)
    projected = jnp.einsum("tc,cjhd->jhtd", row_tokens, mapping, preferred_element_type=jnp.float32)
    multiplier = lax.dynamic_slice_in_dim(logit_multiplier, half * heads_here, heads_here)
    q_items = (projected[0] * multiplier[:, None, None]).astype(jnp.bfloat16)
    k_items = projected[1].astype(jnp.bfloat16)
    v_items = projected[2].astype(jnp.bfloat16)
    per_device = heads_here
    attended = attend(q_items, k_items, v_items)
    attended = attended.reshape(per_device, sectors, tokens, per_group_channel_count)
    attended = jnp.transpose(attended, (1, 0, 2, 3))
    attended = lax.all_to_all(attended, "lon", 0, 0, tiled=True)
    attended = attended.reshape(rows, HEADS, tokens, per_group_channel_count)
    joined = jnp.transpose(attended, (0, 2, 1, 3)).reshape(rows, tokens, widths)
    mixed_out = jnp.dot(joined, mixing_return_matrix, preferred_element_type=jnp.float32)
    return (upcast + mixed_out).astype(jnp.bfloat16)


def solution(mesh):
    return jax.shard_map(
        on_device,
        mesh=mesh,
        in_specs=(P("lat", None, "lon"), P(), P(), P(), P(), P(), P(), P(), P(), P(), P()),
        out_specs=P("lat", "lon", None),
        check_vma=False,
    )
```

```python
import jax
import jax.numpy as jnp
from jax import lax
from jax.sharding import PartitionSpec as P

HEADS = 8
HALO = 4


def extend_lat(value, width):
    size, length = lax.axis_size("lat"), value.shape[0]
    up = [(i, i + 1) for i in range(size - 1)]
    down = [(i + 1, i) for i in range(size - 1)]
    source = lax.optimization_barrier(value)
    before = lax.ppermute(source[length - width :], "lat", up)
    after = lax.ppermute(source[:width], "lat", down)
    return jnp.concatenate([before, value, after], axis=0)


def extend_lon(value, width, dim):
    size, length = lax.axis_size("lon"), value.shape[dim]
    up = [(i, (i + 1) % size) for i in range(size)]
    down = [(j, i) for i, j in up]
    last = lax.slice_in_dim(value, length - width, length, axis=dim)
    initial = lax.slice_in_dim(value, 0, width, axis=dim)
    before = lax.ppermute(last, "lon", up)
    after = lax.ppermute(initial, "lon", down)
    return jnp.concatenate([before, value, after], axis=dim)


def clear_outside(value, start, total):
    count = value.shape[0]
    rows = start + jnp.arange(count)
    keep = (rows >= 0) & (rows < total)
    shape = (count,) + (1,) * (value.ndim - 1)
    return jnp.where(keep.reshape(shape), value, jnp.zeros_like(value))


def first_conv(extended, kernel, bias):
    total = lax.conv_general_dilated(
        extended[None],
        kernel,
        (1, 1),
        "VALID",
        dimension_numbers=("NHCW", "HWIO", "NHWC"),
        preferred_element_type=jnp.float32,
    )[0]
    return jax.nn.silu(total + bias).astype(jnp.bfloat16)


def halving_filter(extended, kernel, bias):
    total = lax.conv_general_dilated(
        extended[None],
        kernel,
        (2, 2),
        "VALID",
        dimension_numbers=("NHWC", "HWIO", "NHWC"),
        preferred_element_type=jnp.float32,
    )[0]
    return jax.nn.silu(total + bias).astype(jnp.bfloat16)


def on_device(
    meridian_slab_data,
    smoothing_filter_taps,
    smoothing_offset_entries,
    opening_coarsen_taps,
    opening_coarsen_offset,
    closing_coarsen_taps,
    closing_coarsen_offset,
    layernorm_multiplier,
    triple_mapping_matrix,
    logit_sharpness,
    mixing_return_matrix,
):
    band = meridian_slab_data.shape[0]
    lat_total = band * lax.axis_size("lat")
    base = lax.axis_index("lat") * band
    extended = extend_lat(meridian_slab_data, HALO)
    extended = extend_lon(extended, HALO, 2)
    opening_halved = first_conv(extended, smoothing_filter_taps, smoothing_offset_entries)
    opening_halved = clear_outside(opening_halved, base - HALO + 1, lat_total)
    closing_halved = halving_filter(opening_halved, opening_coarsen_taps, opening_coarsen_offset)
    count = closing_halved.shape[0]
    first_row = base // 2 - 1
    keep_top = (first_row >= 0).astype(closing_halved.dtype)
    keep_bottom = (first_row + count - 1 < lat_total // 2).astype(closing_halved.dtype)
    closing_halved = jnp.concatenate(
        [closing_halved[:1] * keep_top, closing_halved[1:-1], closing_halved[-1:] * keep_bottom], axis=0
    )
    activation_maps = halving_filter(
        closing_halved, closing_coarsen_taps, closing_coarsen_offset
    )
    rows, tokens, widths = activation_maps.shape
    per_group_channel_count = widths // HEADS
    upcast = activation_maps.astype(jnp.float32)
    mean = jnp.mean(upcast, axis=-1, keepdims=True)
    centred = upcast - mean
    variance = jnp.mean(centred * centred, axis=-1, keepdims=True)
    normed = (centred * lax.rsqrt(variance + 1e-05) * layernorm_multiplier).astype(jnp.bfloat16)
    d = widths // HEADS
    logit_multiplier = logit_sharpness / jnp.sqrt(jnp.float32(d))

    sectors = lax.axis_size("lon")
    per_row = sectors // rows
    heads_here = HEADS // per_row
    half = lax.axis_index("lon") % per_row
    row_copies = jnp.repeat(normed, per_row, axis=0)
    gathered = lax.all_to_all(row_copies, "lon", 0, 0, tiled=True)
    row_tokens = gathered.reshape(sectors * tokens, widths)
    mapping = triple_mapping_matrix.reshape(widths, 3, HEADS, d)
    mapping = lax.dynamic_slice_in_dim(mapping, half * heads_here, heads_here, axis=2)
    projected = jnp.einsum("tc,cjhd->jhtd", row_tokens, mapping, preferred_element_type=jnp.float32)
    multiplier = lax.dynamic_slice_in_dim(logit_multiplier, half * heads_here, heads_here)
    q_items = (projected[0] * multiplier[:, None, None]).astype(jnp.bfloat16)
    k_items = projected[1].astype(jnp.bfloat16)
    v_items = projected[2].astype(jnp.bfloat16)
    per_device = heads_here
    scores = jnp.einsum("isd,itd->ist", q_items, k_items, preferred_element_type=jnp.float32)
    best = jnp.max(scores, axis=-1, keepdims=True)
    weights = jnp.exp(scores - best)
    total = jnp.sum(weights, axis=-1, keepdims=True)
    summed = jnp.einsum(
        "ist,itd->isd", weights.astype(jnp.bfloat16), v_items, preferred_element_type=jnp.float32
    )
    attended = (summed / total).astype(jnp.bfloat16)
    attended = attended.reshape(per_device, sectors, tokens, per_group_channel_count)
    attended = jnp.transpose(attended, (1, 0, 2, 3))
    attended = lax.all_to_all(attended, "lon", 0, 0, tiled=True)
    attended = attended.reshape(rows, HEADS, tokens, per_group_channel_count)
    joined = jnp.transpose(attended, (0, 2, 1, 3)).reshape(rows, tokens, widths)
    mixed_out = jnp.dot(joined, mixing_return_matrix, preferred_element_type=jnp.float32)
    return (upcast + mixed_out).astype(jnp.bfloat16)


def solution(mesh):
    return jax.shard_map(
        on_device,
        mesh=mesh,
        in_specs=(P("lat", None, "lon"), P(), P(), P(), P(), P(), P(), P(), P(), P(), P()),
        out_specs=P("lat", "lon", None),
        check_vma=False,
    )
```

```python
import jax
import jax.numpy as jnp
from jax import lax
from jax.sharding import PartitionSpec as P

HEADS = 8
HALO = 4


def extend_lat(value, width):
    size, length = lax.axis_size("lat"), value.shape[0]
    up = [(i, i + 1) for i in range(size - 1)]
    down = [(i + 1, i) for i in range(size - 1)]
    source = lax.optimization_barrier(value)
    before = lax.ppermute(source[length - width :], "lat", up)
    after = lax.ppermute(source[:width], "lat", down)
    return jnp.concatenate([before, value, after], axis=0)


def extend_lon(value, width, dim):
    size, length = lax.axis_size("lon"), value.shape[dim]
    up = [(i, (i + 1) % size) for i in range(size)]
    down = [(j, i) for i, j in up]
    last = lax.slice_in_dim(value, length - width, length, axis=dim)
    initial = lax.slice_in_dim(value, 0, width, axis=dim)
    before = lax.ppermute(last, "lon", up)
    after = lax.ppermute(initial, "lon", down)
    return jnp.concatenate([before, value, after], axis=dim)


def clear_outside(value, start, total):
    count = value.shape[0]
    rows = start + jnp.arange(count)
    keep = (rows >= 0) & (rows < total)
    shape = (count,) + (1,) * (value.ndim - 1)
    return jnp.where(keep.reshape(shape), value, jnp.zeros_like(value))


def first_conv(extended, kernel, bias):
    total = lax.conv_general_dilated(
        extended[None],
        kernel,
        (1, 1),
        "VALID",
        dimension_numbers=("NHCW", "HWIO", "NHWC"),
        preferred_element_type=jnp.float32,
    )[0]
    return jax.nn.silu(total + bias).astype(jnp.bfloat16)


def halving_filter(extended, kernel, bias):
    total = lax.conv_general_dilated(
        extended[None],
        kernel,
        (2, 2),
        "VALID",
        dimension_numbers=("NHWC", "HWIO", "NHWC"),
        preferred_element_type=jnp.float32,
    )[0]
    return jax.nn.silu(total + bias).astype(jnp.bfloat16)


def on_device(
    meridian_slab_data,
    smoothing_filter_taps,
    smoothing_offset_entries,
    opening_coarsen_taps,
    opening_coarsen_offset,
    closing_coarsen_taps,
    closing_coarsen_offset,
    layernorm_multiplier,
    triple_mapping_matrix,
    logit_sharpness,
    mixing_return_matrix,
):
    band = meridian_slab_data.shape[0]
    lat_total = band * lax.axis_size("lat")
    base = lax.axis_index("lat") * band
    n_lat, n_lon = lax.axis_size("lat"), lax.axis_size("lon")
    width = meridian_slab_data.shape[2]
    source = lax.optimization_barrier(meridian_slab_data)
    left = lax.ppermute(source[:, :, width - HALO :], "lon", [(i, (i + 1) % n_lon) for i in range(n_lon)])
    right = lax.ppermute(source[:, :, :HALO], "lon", [((i + 1) % n_lon, i) for i in range(n_lon)])
    wide = jnp.concatenate([left, meridian_slab_data, right], axis=2)
    top = lax.ppermute(wide[band - HALO :], "lat", [(i, i + 1) for i in range(n_lat - 1)])
    bottom = lax.ppermute(wide[:HALO], "lat", [(i + 1, i) for i in range(n_lat - 1)])
    middle = first_conv(wide, smoothing_filter_taps, smoothing_offset_entries)
    upper = first_conv(jnp.concatenate([top, wide[:2]], axis=0), smoothing_filter_taps, smoothing_offset_entries)
    lower = first_conv(jnp.concatenate([wide[band - 2 :], bottom], axis=0), smoothing_filter_taps, smoothing_offset_entries)
    opening_halved = jnp.concatenate([upper, middle, lower], axis=0)
    opening_halved = clear_outside(opening_halved, base - HALO + 1, lat_total)
    closing_halved = halving_filter(opening_halved, opening_coarsen_taps, opening_coarsen_offset)
    closing_halved = clear_outside(closing_halved, base // 2 - 1, lat_total // 2)
    closing_halved = lax.optimization_barrier(closing_halved)
    activation_maps = halving_filter(
        closing_halved, closing_coarsen_taps, closing_coarsen_offset
    )
    rows, tokens, widths = activation_maps.shape
    per_group_channel_count = widths // HEADS
    upcast = activation_maps.astype(jnp.float32)
    mean = jnp.mean(upcast, axis=-1, keepdims=True)
    centred = upcast - mean
    variance = jnp.mean(centred * centred, axis=-1, keepdims=True)
    normed = (centred * lax.rsqrt(variance + 1e-05) * layernorm_multiplier).astype(jnp.bfloat16)
    d = widths // HEADS
    logit_multiplier = logit_sharpness / jnp.sqrt(jnp.float32(d))

    sectors = lax.axis_size("lon")
    per_row = sectors // rows
    heads_here = HEADS // per_row
    half = lax.axis_index("lon") % per_row
    row_copies = jnp.repeat(normed, per_row, axis=0)
    gathered = lax.all_to_all(row_copies, "lon", 0, 0, tiled=True)
    row_tokens = gathered.reshape(sectors * tokens, widths)
    mapping = triple_mapping_matrix.reshape(widths, 3, HEADS, d)
    mapping = lax.dynamic_slice_in_dim(mapping, half * heads_here, heads_here, axis=2)
    projected = jnp.einsum("tc,cjhd->jhtd", row_tokens, mapping, preferred_element_type=jnp.float32)
    multiplier = lax.dynamic_slice_in_dim(logit_multiplier, half * heads_here, heads_here)
    q_items = (projected[0] * multiplier[:, None, None]).astype(jnp.bfloat16)
    k_items = projected[1].astype(jnp.bfloat16)
    v_items = projected[2].astype(jnp.bfloat16)
    per_device = heads_here
    scores = jnp.einsum("isd,itd->ist", q_items, k_items, preferred_element_type=jnp.float32)
    best = jnp.max(scores, axis=-1, keepdims=True)
    weights = jnp.exp(scores - best)
    total = jnp.sum(weights, axis=-1, keepdims=True)
    summed = jnp.einsum(
        "ist,itd->isd", weights.astype(jnp.bfloat16), v_items, preferred_element_type=jnp.float32
    )
    attended = (summed / total).astype(jnp.bfloat16)
    attended = attended.reshape(per_device, sectors, tokens, per_group_channel_count)
    attended = jnp.transpose(attended, (1, 0, 2, 3))
    attended = lax.all_to_all(attended, "lon", 0, 0, tiled=True)
    attended = attended.reshape(rows, HEADS, tokens, per_group_channel_count)
    joined = jnp.transpose(attended, (0, 2, 1, 3)).reshape(rows, tokens, widths)
    mixed_out = jnp.dot(joined, mixing_return_matrix, preferred_element_type=jnp.float32)
    return (upcast + mixed_out).astype(jnp.bfloat16)


def solution(mesh):
    return jax.shard_map(
        on_device,
        mesh=mesh,
        in_specs=(P("lat", None, "lon"), P(), P(), P(), P(), P(), P(), P(), P(), P(), P()),
        out_specs=P("lat", "lon", None),
        check_vma=False,
    )
```

```python
import jax
import jax.numpy as jnp
from jax import lax
from jax.sharding import PartitionSpec as P

HEADS = 8
HALO = 4


def extend_lat(value, width):
    size, length = lax.axis_size("lat"), value.shape[0]
    up = [(i, i + 1) for i in range(size - 1)]
    down = [(i + 1, i) for i in range(size - 1)]
    source = lax.optimization_barrier(value)
    before = lax.ppermute(source[length - width :], "lat", up)
    after = lax.ppermute(source[:width], "lat", down)
    return jnp.concatenate([before, value, after], axis=0)


def extend_lon(value, width, dim):
    size, length = lax.axis_size("lon"), value.shape[dim]
    up = [(i, (i + 1) % size) for i in range(size)]
    down = [(j, i) for i, j in up]
    last = lax.slice_in_dim(value, length - width, length, axis=dim)
    initial = lax.slice_in_dim(value, 0, width, axis=dim)
    before = lax.ppermute(last, "lon", up)
    after = lax.ppermute(initial, "lon", down)
    return jnp.concatenate([before, value, after], axis=dim)


def clear_outside(value, start, total):
    count = value.shape[0]
    rows = start + jnp.arange(count)
    keep = (rows >= 0) & (rows < total)
    shape = (count,) + (1,) * (value.ndim - 1)
    return jnp.where(keep.reshape(shape), value, jnp.zeros_like(value))


def first_conv(extended, kernel, bias):
    total = lax.conv_general_dilated(
        extended[None],
        kernel,
        (1, 1),
        "VALID",
        dimension_numbers=("NHCW", "HWIO", "NHWC"),
        preferred_element_type=jnp.float32,
    )[0]
    return jax.nn.silu(total + bias).astype(jnp.bfloat16)


def halving_filter(extended, kernel, bias):
    total = lax.conv_general_dilated(
        extended[None],
        kernel,
        (2, 2),
        "VALID",
        dimension_numbers=("NHWC", "HWIO", "NHWC"),
        preferred_element_type=jnp.float32,
    )[0]
    return jax.nn.silu(total + bias).astype(jnp.bfloat16)


def on_device(
    meridian_slab_data,
    smoothing_filter_taps,
    smoothing_offset_entries,
    opening_coarsen_taps,
    opening_coarsen_offset,
    closing_coarsen_taps,
    closing_coarsen_offset,
    layernorm_multiplier,
    triple_mapping_matrix,
    logit_sharpness,
    mixing_return_matrix,
):
    band = meridian_slab_data.shape[0]
    lat_total = band * lax.axis_size("lat")
    base = lax.axis_index("lat") * band
    n_lat, n_lon = lax.axis_size("lat"), lax.axis_size("lon")
    width = meridian_slab_data.shape[2]
    source = lax.optimization_barrier(meridian_slab_data)
    left = lax.ppermute(source[:, :, width - HALO :], "lon", [(i, (i + 1) % n_lon) for i in range(n_lon)])
    right = lax.ppermute(source[:, :, :HALO], "lon", [((i + 1) % n_lon, i) for i in range(n_lon)])
    wide = jnp.concatenate([left, meridian_slab_data, right], axis=2)
    top = lax.ppermute(wide[band - HALO :], "lat", [(i, i + 1) for i in range(n_lat - 1)])
    bottom = lax.ppermute(wide[:HALO], "lat", [(i + 1, i) for i in range(n_lat - 1)])
    middle = first_conv(wide, smoothing_filter_taps, smoothing_offset_entries)
    upper = first_conv(jnp.concatenate([top, wide[:2]], axis=0), smoothing_filter_taps, smoothing_offset_entries)
    lower = first_conv(jnp.concatenate([wide[band - 2 :], bottom], axis=0), smoothing_filter_taps, smoothing_offset_entries)
    upper = clear_outside(upper, base - HALO + 1, lat_total)
    lower = clear_outside(lower, base + band - 1, lat_total)
    opening_halved = jnp.concatenate([upper, middle, lower], axis=0)
    closing_halved = halving_filter(opening_halved, opening_coarsen_taps, opening_coarsen_offset)
    closing_halved = clear_outside(closing_halved, base // 2 - 1, lat_total // 2)
    closing_halved = lax.optimization_barrier(closing_halved)
    activation_maps = halving_filter(
        closing_halved, closing_coarsen_taps, closing_coarsen_offset
    )
    rows, tokens, widths = activation_maps.shape
    per_group_channel_count = widths // HEADS
    upcast = activation_maps.astype(jnp.float32)
    mean = jnp.mean(upcast, axis=-1, keepdims=True)
    centred = upcast - mean
    variance = jnp.mean(centred * centred, axis=-1, keepdims=True)
    normed = (centred * lax.rsqrt(variance + 1e-05) * layernorm_multiplier).astype(jnp.bfloat16)
    d = widths // HEADS
    logit_multiplier = logit_sharpness / jnp.sqrt(jnp.float32(d))

    sectors = lax.axis_size("lon")
    per_row = sectors // rows
    heads_here = HEADS // per_row
    half = lax.axis_index("lon") % per_row
    row_copies = jnp.repeat(normed, per_row, axis=0)
    gathered = lax.all_to_all(row_copies, "lon", 0, 0, tiled=True)
    row_tokens = gathered.reshape(sectors * tokens, widths)
    mapping = triple_mapping_matrix.reshape(widths, 3, HEADS, d)
    mapping = lax.dynamic_slice_in_dim(mapping, half * heads_here, heads_here, axis=2)
    projected = jnp.einsum("tc,cjhd->jhtd", row_tokens, mapping, preferred_element_type=jnp.float32)
    multiplier = lax.dynamic_slice_in_dim(logit_multiplier, half * heads_here, heads_here)
    q_items = (projected[0] * multiplier[:, None, None]).astype(jnp.bfloat16)
    k_items = projected[1].astype(jnp.bfloat16)
    v_items = projected[2].astype(jnp.bfloat16)
    per_device = heads_here
    scores = jnp.einsum("isd,itd->ist", q_items, k_items, preferred_element_type=jnp.float32)
    best = jnp.max(scores, axis=-1, keepdims=True)
    weights = jnp.exp(scores - best)
    total = jnp.sum(weights, axis=-1, keepdims=True)
    summed = jnp.einsum(
        "ist,itd->isd", weights.astype(jnp.bfloat16), v_items, preferred_element_type=jnp.float32
    )
    attended = (summed / total).astype(jnp.bfloat16)
    attended = attended.reshape(per_device, sectors, tokens, per_group_channel_count)
    attended = jnp.transpose(attended, (1, 0, 2, 3))
    attended = lax.all_to_all(attended, "lon", 0, 0, tiled=True)
    attended = attended.reshape(rows, HEADS, tokens, per_group_channel_count)
    joined = jnp.transpose(attended, (0, 2, 1, 3)).reshape(rows, tokens, widths)
    mixed_out = jnp.dot(joined, mixing_return_matrix, preferred_element_type=jnp.float32)
    return (upcast + mixed_out).astype(jnp.bfloat16)


def solution(mesh):
    return jax.shard_map(
        on_device,
        mesh=mesh,
        in_specs=(P("lat", None, "lon"), P(), P(), P(), P(), P(), P(), P(), P(), P(), P()),
        out_specs=P("lat", "lon", None),
        check_vma=False,
    )
```

```python
import jax
import jax.numpy as jnp
from jax import lax
from jax.sharding import PartitionSpec as P

HEADS = 8
HALO = 4


def extend_lat(value, width):
    size, length = lax.axis_size("lat"), value.shape[0]
    up = [(i, i + 1) for i in range(size - 1)]
    down = [(i + 1, i) for i in range(size - 1)]
    source = lax.optimization_barrier(value)
    before = lax.ppermute(source[length - width :], "lat", up)
    after = lax.ppermute(source[:width], "lat", down)
    return jnp.concatenate([before, value, after], axis=0)


def extend_lon(value, width, dim):
    size, length = lax.axis_size("lon"), value.shape[dim]
    up = [(i, (i + 1) % size) for i in range(size)]
    down = [(j, i) for i, j in up]
    last = lax.slice_in_dim(value, length - width, length, axis=dim)
    initial = lax.slice_in_dim(value, 0, width, axis=dim)
    before = lax.ppermute(last, "lon", up)
    after = lax.ppermute(initial, "lon", down)
    return jnp.concatenate([before, value, after], axis=dim)


def clear_outside(value, start, total):
    count = value.shape[0]
    rows = start + jnp.arange(count)
    keep = (rows >= 0) & (rows < total)
    shape = (count,) + (1,) * (value.ndim - 1)
    return jnp.where(keep.reshape(shape), value, jnp.zeros_like(value))


def first_conv(extended, kernel, bias):
    total = lax.conv_general_dilated(
        extended[None],
        kernel,
        (1, 1),
        "VALID",
        dimension_numbers=("NHCW", "HWIO", "NHWC"),
        preferred_element_type=jnp.float32,
    )[0]
    return jax.nn.silu(total + bias).astype(jnp.bfloat16)


def halving_filter(extended, kernel, bias):
    total = lax.conv_general_dilated(
        extended[None],
        kernel,
        (2, 2),
        "VALID",
        dimension_numbers=("NHWC", "HWIO", "NHWC"),
        preferred_element_type=jnp.float32,
    )[0]
    return jax.nn.silu(total + bias).astype(jnp.bfloat16)


def on_device(
    meridian_slab_data,
    smoothing_filter_taps,
    smoothing_offset_entries,
    opening_coarsen_taps,
    opening_coarsen_offset,
    closing_coarsen_taps,
    closing_coarsen_offset,
    layernorm_multiplier,
    triple_mapping_matrix,
    logit_sharpness,
    mixing_return_matrix,
):
    band = meridian_slab_data.shape[0]
    lat_total = band * lax.axis_size("lat")
    base = lax.axis_index("lat") * band
    n_lat, n_lon = lax.axis_size("lat"), lax.axis_size("lon")
    width = meridian_slab_data.shape[2]
    left = lax.ppermute(meridian_slab_data[:, :, width - HALO :], "lon", [(i, (i + 1) % n_lon) for i in range(n_lon)])
    right = lax.ppermute(meridian_slab_data[:, :, :HALO], "lon", [((i + 1) % n_lon, i) for i in range(n_lon)])
    wide = jnp.concatenate([left, meridian_slab_data, right], axis=2)
    top = lax.ppermute(wide[band - HALO :], "lat", [(i, i + 1) for i in range(n_lat - 1)])
    bottom = lax.ppermute(wide[:HALO], "lat", [(i + 1, i) for i in range(n_lat - 1)])
    middle = first_conv(wide, smoothing_filter_taps, smoothing_offset_entries)
    upper = first_conv(jnp.concatenate([top, wide[:2]], axis=0), smoothing_filter_taps, smoothing_offset_entries)
    lower = first_conv(jnp.concatenate([wide[band - 2 :], bottom], axis=0), smoothing_filter_taps, smoothing_offset_entries)
    opening_halved = jnp.concatenate([upper, middle, lower], axis=0)
    opening_halved = clear_outside(opening_halved, base - HALO + 1, lat_total)
    closing_halved = halving_filter(opening_halved, opening_coarsen_taps, opening_coarsen_offset)
    closing_halved = clear_outside(closing_halved, base // 2 - 1, lat_total // 2)
    closing_halved = lax.optimization_barrier(closing_halved)
    activation_maps = halving_filter(
        closing_halved, closing_coarsen_taps, closing_coarsen_offset
    )
    rows, tokens, widths = activation_maps.shape
    per_group_channel_count = widths // HEADS
    upcast = activation_maps.astype(jnp.float32)
    mean = jnp.mean(upcast, axis=-1, keepdims=True)
    centred = upcast - mean
    variance = jnp.mean(centred * centred, axis=-1, keepdims=True)
    normed = (centred * lax.rsqrt(variance + 1e-05) * layernorm_multiplier).astype(jnp.bfloat16)
    d = widths // HEADS
    logit_multiplier = logit_sharpness / jnp.sqrt(jnp.float32(d))

    sectors = lax.axis_size("lon")
    per_row = sectors // rows
    heads_here = HEADS // per_row
    half = lax.axis_index("lon") % per_row
    row_copies = jnp.repeat(normed, per_row, axis=0)
    gathered = lax.all_to_all(row_copies, "lon", 0, 0, tiled=True)
    row_tokens = gathered.reshape(sectors * tokens, widths)
    mapping = triple_mapping_matrix.reshape(widths, 3, HEADS, d)
    mapping = lax.dynamic_slice_in_dim(mapping, half * heads_here, heads_here, axis=2)
    projected = jnp.einsum("tc,cjhd->jhtd", row_tokens, mapping, preferred_element_type=jnp.float32)
    multiplier = lax.dynamic_slice_in_dim(logit_multiplier, half * heads_here, heads_here)
    q_items = (projected[0] * multiplier[:, None, None]).astype(jnp.bfloat16)
    k_items = projected[1].astype(jnp.bfloat16)
    v_items = projected[2].astype(jnp.bfloat16)
    per_device = heads_here
    scores = jnp.einsum("isd,itd->ist", q_items, k_items, preferred_element_type=jnp.float32)
    best = jnp.max(scores, axis=-1, keepdims=True)
    weights = jnp.exp(scores - best)
    total = jnp.sum(weights, axis=-1, keepdims=True)
    summed = jnp.einsum(
        "ist,itd->isd", weights.astype(jnp.bfloat16), v_items, preferred_element_type=jnp.float32
    )
    attended = (summed / total).astype(jnp.bfloat16)
    attended = attended.reshape(per_device, sectors, tokens, per_group_channel_count)
    attended = jnp.transpose(attended, (1, 0, 2, 3))
    attended = lax.all_to_all(attended, "lon", 0, 0, tiled=True)
    attended = attended.reshape(rows, HEADS, tokens, per_group_channel_count)
    joined = jnp.transpose(attended, (0, 2, 1, 3)).reshape(rows, tokens, widths)
    mixed_out = jnp.dot(joined, mixing_return_matrix, preferred_element_type=jnp.float32)
    return (upcast + mixed_out).astype(jnp.bfloat16)


def solution(mesh):
    return jax.shard_map(
        on_device,
        mesh=mesh,
        in_specs=(P("lat", None, "lon"), P(), P(), P(), P(), P(), P(), P(), P(), P(), P()),
        out_specs=P("lat", "lon", None),
        check_vma=False,
    )
```
